32 devices in a mesh: basis: 2 (over x), eig: 8 (over z, y), chan: 2 (over core).
Axes of the slice: x: 2, y: 2, z: 4, core: 2. Of those that a mesh axis runs over, the one named last changes fastest.
Arguments:
- eigvecs: bfloat16 [512, 5120], P('eig', 'basis'), may hold values from -6 to 6
- boundary: bfloat16 [5120, 4096], P('basis', 'chan'), may hold values from -0.3125 to 0.3125
- block_sizes: int32 [16], replicated, may hold values from 256 to 768, as said below
- target_of_channel: int32 [4096], P('chan'), may hold values from 0 to 15, as said below
- poles: float32 [512], replicated, may hold values from -4 to 4, as said below
- energies: float32 [16], P('basis'), may hold values from -0.25 to 0.25
Outputs:
- rmatrix: float32 [16, 4096, 4096], P('basis', 'chan', 'eig')
The draws below stay inside these ranges and needn't reach their ends.
Inputs may be any that keep to these rules, and one draw needn't show every extreme that they name: `poles`: every pole lies 0.5 or more away from zero, with both signs present. `block_sizes`: the sizes sum to 5120; every target state's block holds at least 256 basis rows. `target_of_channel`: every target state has exactly 256 channels.
All inputs are finite; a program needn't handle non-finite values.
Results may differ from the reference program's by a relative error of at most 0.0049.
Values may be sent and summed in bfloat16 or wider, within the bound.
No kernel may reach another device: no remote copies, remote signals or barrier semaphores. Data moves between devices by JAX's collectives and lax.ppermute only.
A program may use at most 128 MiB of HBM per device.

```python
import jax
import jax.numpy as jnp
from jax import lax

C = 4096
NT = 16
K = 512
NB = 5120
NE = 16
LEAST = 256
MOST = 768


def draw_poles(key, part):
    sign_key, size_key = jax.random.split(jax.random.fold_in(key, 11))
    signs = jnp.where(jax.random.randint(sign_key, (K,), 0, 2) == 1, 1.0, -1.0).astype(jnp.float32)
    sizes_drawn = jnp.exp(jax.random.uniform(size_key, (K,), jnp.float32, jnp.log(0.5), jnp.log(4.0)))
    return (signs * sizes_drawn).astype(jnp.float32)


def draw_block_sizes(key, part):
    cut_key, pick_key = jax.random.split(jax.random.fold_in(key, 23))
    half_share = MOST - LEAST
    rest_share = NB - C - half_share
    cuts = jnp.sort(jax.random.randint(cut_key, (NT - 2,), 0, rest_share + 1).astype(jnp.int32))
    edges = jnp.concatenate([jnp.zeros((1,), jnp.int32), cuts, jnp.full((1,), rest_share, jnp.int32)])
    others = edges[1:] - edges[:-1]
    special = jax.random.randint(pick_key, (), 0, NT).astype(jnp.int32)
    slots = jnp.arange(NT, dtype=jnp.int32)
    position = jnp.clip(slots - (slots > special).astype(jnp.int32), 0, NT - 2)
    shares = jnp.where(slots == special, half_share, others[position])
    return (LEAST + shares).astype(jnp.int32)


def draw_target_of_channel(key, part):
    order = jax.random.permutation(jax.random.fold_in(key, 37), C)
    return (order // LEAST).astype(jnp.int32)


def block_levels(key, extent, pieces, low, top_value):
    loudness = 1.0
    for dim, blocks in pieces:
        heights = jax.random.uniform(jax.random.fold_in(jax.random.fold_in(key, 6), dim), (blocks,), jnp.float32, low / len(pieces), top_value / len(pieces))
        loudness = loudness * jnp.repeat(jnp.exp(heights), extent[dim] // blocks).reshape((-1,) + (1,) * (len(extent) - 1 - dim))
    return loudness


def bell_draw(stream_key, extent, scale, most, shards=(), kind=jnp.bfloat16):
    values = jax.random.normal(stream_key, extent, jnp.float32) * scale
    if len(shards) > 0:
        values = block_levels(stream_key, extent, shards, -0.22, 0.18) * values
    return jnp.clip(values, min=-most, max=most).astype(kind)


def setup_inputs(seed: int = 0) -> dict:
    streams_of = jax.random.split(jax.random.key(seed), 7)
    eigvecs = bell_draw(streams_of[0], (K, NB), 1.0, 6.0, ((0, 8), (1, 2)))
    boundary = bell_draw(streams_of[1], (NB, C), (NB // NT) ** -0.5, 0.3125, ((0, 2), (1, 2)))
    block_sizes = draw_block_sizes(jax.random.fold_in(streams_of[6], 71), 0)
    target_of_channel = draw_target_of_channel(jax.random.fold_in(streams_of[6], 71), 0)
    poles = draw_poles(jax.random.fold_in(streams_of[6], 71), 0)
    energies = jnp.clip(jax.random.uniform(streams_of[5], (NE,), jnp.float32, -0.25, 0.25) * block_levels(streams_of[5], (NE,), ((0, 2),), -0.4, 0.0), -0.25, 0.25)
    return dict(eigvecs=eigvecs, boundary=boundary, block_sizes=block_sizes, target_of_channel=target_of_channel, poles=poles, energies=energies)


def reference(eigvecs, boundary, block_sizes, target_of_channel, poles, energies):
    block_ends = jnp.cumsum(block_sizes).astype(jnp.int32)
    row_ids = jnp.arange(NB, dtype=jnp.int32)
    owner_of = jnp.sum((block_ends[None, :] <= row_ids[:, None]).astype(jnp.int32), axis=1).astype(jnp.int32)
    member = owner_of[:, None] == target_of_channel[None, :]
    masked = jnp.where(member, boundary, jnp.zeros_like(boundary))
    amplitudes = jnp.dot(eigvecs, masked, preferred_element_type=jnp.float32).astype(jnp.bfloat16)
    weights = 1.0 / (poles[None, :] - energies[:, None])
    factor = K ** -0.5

    def per_energy(weight_row):
        scaled = (weight_row[:, None] * amplitudes.astype(jnp.float32)).astype(jnp.bfloat16)
        return jnp.dot(scaled.T, amplitudes, preferred_element_type=jnp.float32) * factor

    return lax.map(per_energy, weights)
```

```python
import jax
import jax.numpy as jnp
from jax import lax
from jax.sharding import PartitionSpec as P


def per_device(eigvecs, boundary, block_sizes, target_of_channel, poles, energies):
    n_basis = lax.axis_size("basis")
    n_eig = lax.axis_size("eig")
    n_chan = lax.axis_size("chan")
    rows_here = eigvecs.shape[1]
    block_ends = jnp.cumsum(block_sizes)
    row_ids = lax.axis_index("basis") * rows_here + jnp.arange(rows_here, dtype=jnp.int32)
    owner_of = jnp.sum((block_ends[None, :] <= row_ids[:, None]).astype(jnp.int32), axis=1)
    member = owner_of[:, None] == target_of_channel[None, :]
    masked = jnp.where(member, boundary, jnp.zeros_like(boundary))
    partial_value = jnp.dot(eigvecs, masked, preferred_element_type=jnp.float32)
    summed_rows = lax.psum_scatter(partial_value, "basis", scatter_dimension=0, tiled=True)
    amp_rows = summed_rows.astype(jnp.bfloat16)
    left_panel = lax.all_gather(amp_rows, ("eig", "basis"), axis=0, tiled=True)
    own_width = left_panel.shape[1]
    col_width = own_width * n_chan // n_eig
    ratio = n_eig // n_chan
    eig_index = lax.axis_index("eig")
    piece = lax.dynamic_slice_in_dim(left_panel, (eig_index % ratio) * col_width, col_width, 1)
    pieces = lax.all_gather(piece, "chan", axis=0, tiled=False)
    right_panel = lax.dynamic_index_in_dim(pieces, eig_index // ratio, 0, keepdims=False)
    factor = poles.shape[0] ** (-0.5)
    weights = 1.0 / (poles[None, :] - energies[:, None])
    scaled = (weights[:, :, None] * left_panel[None].astype(jnp.float32)).astype(jnp.bfloat16)
    summed = jnp.einsum("ekc,kd->ecd", scaled, right_panel, preferred_element_type=jnp.float32)
    return summed * factor


def solution(mesh):
    placed = (P("eig", "basis"), P("basis", "chan"), P(), P("chan"), P(), P("basis"))
    return jax.shard_map(
        per_device, mesh=mesh, in_specs=placed, out_specs=P("basis", "chan", "eig"), check_vma=False
    )
```

```python
import jax
import jax.numpy as jnp
import numpy as np
from jax import lax
from jax.sharding import PartitionSpec as P


def ring_order(mesh):
    n = mesh.shape["eig"]
    try:
        index = [0] * len(mesh.axis_names)
        where = mesh.axis_names.index("eig")
        coords = []
        for m in range(n):
            index[where] = m
            coords.append(tuple(int(v) for v in mesh.devices[tuple(index)].coords))
        varying = [a for a in range(len(coords[0])) if len({c[a] for c in coords}) > 1]
        if len(varying) != 2:
            return list(range(n))
        spans = [sorted({c[a] for c in coords}) for a in varying]
        if len(spans[0]) % 2 != 0:
            varying, spans = varying[::-1], spans[::-1]
        rows, cols = spans
        if len(rows) % 2 != 0 or len(cols) < 2 or len(rows) * len(cols) != n:
            return list(range(n))
        at = {(c[varying[0]], c[varying[1]]): m for m, c in enumerate(coords)}
        path = []
        for r_i, r in enumerate(rows):
            tail = cols[1:] if r_i % 2 == 0 else cols[1:][::-1]
            path += [at[(r, c)] for c in tail]
        path += [at[(r, cols[0])] for r in rows[::-1]]
        return path if sorted(path) == list(range(n)) else list(range(n))
    except Exception:
        return list(range(n))


def make_per_device(cycle):
    n_ring = len(cycle)
    position = [0] * n_ring
    for t, m in enumerate(cycle):
        position[m] = t
    fwd_pairs = [(cycle[t], cycle[(t + 1) % n_ring]) for t in range(n_ring)]
    bwd_pairs = [(cycle[t], cycle[(t - 1) % n_ring]) for t in range(n_ring)]
    n_fwd = n_ring // 2
    n_bwd = n_ring - 1 - n_fwd

    def per_device(eigvecs, boundary, block_sizes, target_of_channel, poles, energies):
        n_eig = lax.axis_size("eig")
        n_chan = lax.axis_size("chan")
        rows_here = eigvecs.shape[1]
        block_ends = jnp.cumsum(block_sizes)
        row_ids = lax.axis_index("basis") * rows_here + jnp.arange(rows_here, dtype=jnp.int32)
        owner_of = jnp.sum((block_ends[None, :] <= row_ids[:, None]).astype(jnp.int32), axis=1)
        member = owner_of[:, None] == target_of_channel[None, :]
        masked = jnp.where(member, boundary, jnp.zeros_like(boundary))
        partial_value = jnp.dot(eigvecs, masked, preferred_element_type=jnp.float32)
        n_basis = lax.axis_size("basis")
        total = partial_value
        for s in range(1, n_basis):
            shift = [(b, (b + s) % n_basis) for b in range(n_basis)]
            total = total + lax.ppermute(partial_value, "basis", shift)
        amp = total.astype(jnp.bfloat16)
        eig_index = lax.axis_index("eig")
        cycle_arr = jnp.array(cycle, dtype=jnp.int32)
        pos = jnp.array(position, dtype=jnp.int32)[eig_index]
        k_here = amp.shape[0]
        left_panel = jnp.zeros((k_here * n_ring, amp.shape[1]), amp.dtype)
        left_panel = lax.dynamic_update_slice_in_dim(left_panel, amp, eig_index * k_here, 0)
        fwd, bwd = amp, amp
        for s in range(max(n_fwd, n_bwd)):
            if s < n_fwd:
                fwd = lax.ppermute(fwd, "eig", fwd_pairs)
                origin = cycle_arr[(pos - s - 1) % n_ring]
                left_panel = lax.dynamic_update_slice_in_dim(left_panel, fwd, origin * k_here, 0)
            if s < n_bwd:
                bwd = lax.ppermute(bwd, "eig", bwd_pairs)
                origin = cycle_arr[(pos + s + 1) % n_ring]
                left_panel = lax.dynamic_update_slice_in_dim(left_panel, bwd, origin * k_here, 0)
        own_width = left_panel.shape[1]
        col_width = own_width * n_chan // n_eig
        ratio = n_eig // n_chan
        piece = lax.dynamic_slice_in_dim(left_panel, (eig_index % ratio) * col_width, col_width, 1)
        holder = eig_index // ratio
        if n_chan == 2:
            other = lax.ppermute(piece, "chan", [(0, 1), (1, 0)])
            right_panel = jnp.where(lax.axis_index("chan") == holder, piece, other)
        else:
            pieces = lax.all_gather(piece, "chan", axis=0, tiled=False)
            right_panel = lax.dynamic_index_in_dim(pieces, holder, 0, keepdims=False)
        factor = poles.shape[0] ** (-0.5)
        weights = 1.0 / (poles[None, :] - energies[:, None])
        scaled = (weights[:, :, None] * left_panel[None].astype(jnp.float32)).astype(jnp.bfloat16)
        summed = jnp.einsum("ekc,kd->ecd", scaled, right_panel, preferred_element_type=jnp.float32)
        return summed * factor

    return per_device


def solution(mesh):
    placed = (P("eig", "basis"), P("basis", "chan"), P(), P("chan"), P(), P("basis"))
    return jax.shard_map(
        make_per_device(ring_order(mesh)),
        mesh=mesh,
        in_specs=placed,
        out_specs=P("basis", "chan", "eig"),
        check_vma=False,
    )
```

```python
import jax
import jax.numpy as jnp
import numpy as np
from jax import lax
from jax.experimental import pallas as pl
from jax.experimental.pallas import tpu as pltpu
from jax.sharding import PartitionSpec as P


def ring_order(mesh):
    n = mesh.shape["eig"]
    try:
        index = [0] * len(mesh.axis_names)
        where = mesh.axis_names.index("eig")
        coords = []
        for m in range(n):
            index[where] = m
            coords.append(tuple(int(v) for v in mesh.devices[tuple(index)].coords))
        varying = [a for a in range(len(coords[0])) if len({c[a] for c in coords}) > 1]
        if len(varying) != 2:
            return list(range(n))
        spans = [sorted({c[a] for c in coords}) for a in varying]
        if len(spans[0]) % 2 != 0:
            varying, spans = varying[::-1], spans[::-1]
        rows, cols = spans
        if len(rows) % 2 != 0 or len(cols) < 2 or len(rows) * len(cols) != n:
            return list(range(n))
        at = {(c[varying[0]], c[varying[1]]): m for m, c in enumerate(coords)}
        path = []
        for r_i, r in enumerate(rows):
            tail = cols[1:] if r_i % 2 == 0 else cols[1:][::-1]
            path += [at[(r, c)] for c in tail]
        path += [at[(r, cols[0])] for r in rows[::-1]]
        return path if sorted(path) == list(range(n)) else list(range(n))
    except Exception:
        return list(range(n))


def rmatrix_kernel(factor, w_ref, lt_ref, r_ref, o_ref):
    e = pl.program_id(1)
    w = w_ref[pl.ds(e, 1), :]
    scaled = (lt_ref[...].astype(jnp.float32) * w).astype(jnp.bfloat16)
    o_ref[0] = jnp.dot(scaled, r_ref[...], preferred_element_type=jnp.float32) * factor


def rmatrix(weights, left_t, right_panel, factor):
    n_e, k_all = weights.shape
    width, _ = left_t.shape
    cols = right_panel.shape[1]
    tile = min(512, width)
    return pl.pallas_call(
        lambda *refs: rmatrix_kernel(factor, *refs),
        grid=(width // tile, n_e),
        in_specs=[
            pl.BlockSpec((n_e, k_all), lambda c, e: (0, 0)),
            pl.BlockSpec((tile, k_all), lambda c, e: (c, 0)),
            pl.BlockSpec((k_all, cols), lambda c, e: (0, 0)),
        ],
        out_specs=pl.BlockSpec((1, tile, cols), lambda c, e: (e, c, 0)),
        out_shape=jax.ShapeDtypeStruct((n_e, width, cols), jnp.float32),
        compiler_params=pltpu.CompilerParams(dimension_semantics=("arbitrary", "arbitrary")),
        cost_estimate=pl.CostEstimate(
            flops=2 * n_e * width * k_all * cols,
            bytes_accessed=4 * n_e * width * cols + 2 * width * k_all + 2 * k_all * cols,
            transcendentals=0,
        ),
    )(weights, left_t, right_panel)


def make_per_device(cycle):
    n_ring = len(cycle)
    position = [0] * n_ring
    for t, m in enumerate(cycle):
        position[m] = t
    fwd_pairs = [(cycle[t], cycle[(t + 1) % n_ring]) for t in range(n_ring)]
    bwd_pairs = [(cycle[t], cycle[(t - 1) % n_ring]) for t in range(n_ring)]
    n_fwd = n_ring // 2
    n_bwd = n_ring - 1 - n_fwd

    def per_device(eigvecs, boundary, block_sizes, target_of_channel, poles, energies):
        n_eig = lax.axis_size("eig")
        n_chan = lax.axis_size("chan")
        rows_here = eigvecs.shape[1]
        block_ends = jnp.cumsum(block_sizes)
        row_ids = lax.axis_index("basis") * rows_here + jnp.arange(rows_here, dtype=jnp.int32)
        owner_of = jnp.sum((block_ends[None, :] <= row_ids[:, None]).astype(jnp.int32), axis=1)
        member = owner_of[:, None] == target_of_channel[None, :]
        masked = jnp.where(member, boundary, jnp.zeros_like(boundary))
        partial_value = jnp.dot(eigvecs, masked, preferred_element_type=jnp.float32)
        n_basis = lax.axis_size("basis")
        total = partial_value
        for s in range(1, n_basis):
            shift = [(b, (b + s) % n_basis) for b in range(n_basis)]
            total = total + lax.ppermute(partial_value, "basis", shift)
        amp = total.astype(jnp.bfloat16)
        eig_index = lax.axis_index("eig")
        cycle_arr = jnp.array(cycle, dtype=jnp.int32)
        pos = jnp.array(position, dtype=jnp.int32)[eig_index]
        k_here = amp.shape[0]
        left_panel = jnp.zeros((k_here * n_ring, amp.shape[1]), amp.dtype)
        left_panel = lax.dynamic_update_slice_in_dim(left_panel, amp, eig_index * k_here, 0)
        fwd, bwd = amp, amp
        for s in range(max(n_fwd, n_bwd)):
            if s < n_fwd:
                fwd = lax.ppermute(fwd, "eig", fwd_pairs)
                origin = cycle_arr[(pos - s - 1) % n_ring]
                left_panel = lax.dynamic_update_slice_in_dim(left_panel, fwd, origin * k_here, 0)
            if s < n_bwd:
                bwd = lax.ppermute(bwd, "eig", bwd_pairs)
                origin = cycle_arr[(pos + s + 1) % n_ring]
                left_panel = lax.dynamic_update_slice_in_dim(left_panel, bwd, origin * k_here, 0)
        own_width = left_panel.shape[1]
        col_width = own_width * n_chan // n_eig
        ratio = n_eig // n_chan
        piece = lax.dynamic_slice_in_dim(left_panel, (eig_index % ratio) * col_width, col_width, 1)
        holder = eig_index // ratio
        if n_chan == 2:
            other = lax.ppermute(piece, "chan", [(0, 1), (1, 0)])
            right_panel = jnp.where(lax.axis_index("chan") == holder, piece, other)
        else:
            pieces = lax.all_gather(piece, "chan", axis=0, tiled=False)
            right_panel = lax.dynamic_index_in_dim(pieces, holder, 0, keepdims=False)
        factor = poles.shape[0] ** (-0.5)
        weights = 1.0 / (poles[None, :] - energies[:, None])
        return rmatrix(weights, left_panel.T, right_panel, factor)

    return per_device


def solution(mesh):
    placed = (P("eig", "basis"), P("basis", "chan"), P(), P("chan"), P(), P("basis"))
    return jax.shard_map(
        make_per_device(ring_order(mesh)),
        mesh=mesh,
        in_specs=placed,
        out_specs=P("basis", "chan", "eig"),
        check_vma=False,
    )
```

```python
import jax
import jax.numpy as jnp
import numpy as np
from jax import lax
from jax.sharding import PartitionSpec as P


def ring_order(mesh):
    n = mesh.shape["eig"]
    try:
        index = [0] * len(mesh.axis_names)
        where = mesh.axis_names.index("eig")
        coords = []
        for m in range(n):
            index[where] = m
            coords.append(tuple(int(v) for v in mesh.devices[tuple(index)].coords))
        varying = [a for a in range(len(coords[0])) if len({c[a] for c in coords}) > 1]
        if len(varying) != 2:
            return list(range(n))
        spans = [sorted({c[a] for c in coords}) for a in varying]
        if len(spans[0]) % 2 != 0:
            varying, spans = varying[::-1], spans[::-1]
        rows, cols = spans
        if len(rows) % 2 != 0 or len(cols) < 2 or len(rows) * len(cols) != n:
            return list(range(n))
        at = {(c[varying[0]], c[varying[1]]): m for m, c in enumerate(coords)}
        path = []
        for r_i, r in enumerate(rows):
            tail = cols[1:] if r_i % 2 == 0 else cols[1:][::-1]
            path += [at[(r, c)] for c in tail]
        path += [at[(r, cols[0])] for r in rows[::-1]]
        return path if sorted(path) == list(range(n)) else list(range(n))
    except Exception:
        return list(range(n))


def make_per_device(cycle):
    n_ring = len(cycle)
    position = [0] * n_ring
    for t, m in enumerate(cycle):
        position[m] = t
    fwd_pairs = [(cycle[t], cycle[(t + 1) % n_ring]) for t in range(n_ring)]
    bwd_pairs = [(cycle[t], cycle[(t - 1) % n_ring]) for t in range(n_ring)]
    n_fwd = n_ring // 2
    n_bwd = n_ring - 1 - n_fwd

    def per_device(eigvecs, boundary, block_sizes, target_of_channel, poles, energies):
        n_eig = lax.axis_size("eig")
        n_chan = lax.axis_size("chan")
        rows_here = eigvecs.shape[1]
        block_ends = jnp.cumsum(block_sizes)
        row_ids = lax.axis_index("basis") * rows_here + jnp.arange(rows_here, dtype=jnp.int32)
        owner_of = jnp.sum((block_ends[None, :] <= row_ids[:, None]).astype(jnp.int32), axis=1)
        member = owner_of[:, None] == target_of_channel[None, :]
        masked = jnp.where(member, boundary, jnp.zeros_like(boundary))
        n_basis = lax.axis_size("basis")
        width = masked.shape[1]
        halves = 2 if width % 256 == 0 else 1
        step = width // halves
        amp_parts = []
        for h in range(halves):
            part = jnp.dot(eigvecs, masked[:, h * step:(h + 1) * step], preferred_element_type=jnp.float32)
            total = part
            for s in range(1, n_basis):
                shift = [(b, (b + s) % n_basis) for b in range(n_basis)]
                total = total + lax.ppermute(part, "basis", shift)
            amp_parts.append(total.astype(jnp.bfloat16))
        amp = jnp.concatenate(amp_parts, axis=1) if halves > 1 else amp_parts[0]
        eig_index = lax.axis_index("eig")
        cycle_arr = jnp.array(cycle, dtype=jnp.int32)
        pos = jnp.array(position, dtype=jnp.int32)[eig_index]
        k_here = amp.shape[0]
        col_width = width * n_chan // n_eig
        ratio = n_eig // n_chan
        col_first = (eig_index % ratio) * col_width
        n_e = energies.shape[0]
        scaled_t = jnp.zeros((n_e, width, k_here * n_ring), jnp.bfloat16)
        right_rows = []

        def take(slot, block, origin, scaled_t):
            pole_part = lax.dynamic_slice_in_dim(poles, origin * k_here, k_here)
            weights = 1.0 / (pole_part[None, :] - energies[:, None])
            piece = (weights[:, None, :] * block.T[None].astype(jnp.float32)).astype(jnp.bfloat16)
            scaled_t = scaled_t.at[:, :, slot * k_here:(slot + 1) * k_here].set(piece)
            right_rows.append(lax.dynamic_slice_in_dim(block, col_first, col_width, 1))
            return scaled_t

        scaled_t = take(0, amp, eig_index, scaled_t)
        slot = 1
        fwd, bwd = amp, amp
        for s in range(max(n_fwd, n_bwd)):
            if s < n_fwd:
                fwd = lax.ppermute(fwd, "eig", fwd_pairs)
                scaled_t = take(slot, fwd, cycle_arr[(pos - s - 1) % n_ring], scaled_t)
                slot += 1
            if s < n_bwd:
                bwd = lax.ppermute(bwd, "eig", bwd_pairs)
                scaled_t = take(slot, bwd, cycle_arr[(pos + s + 1) % n_ring], scaled_t)
                slot += 1
        piece = jnp.concatenate(right_rows, axis=0)
        holder = eig_index // ratio
        if n_chan == 2:
            other = lax.ppermute(piece, "chan", [(0, 1), (1, 0)])
            right_panel = jnp.where(lax.axis_index("chan") == holder, piece, other)
        else:
            pieces = lax.all_gather(piece, "chan", axis=0, tiled=False)
            right_panel = lax.dynamic_index_in_dim(pieces, holder, 0, keepdims=False)
        factor = poles.shape[0] ** (-0.5)
        summed = jnp.einsum("eck,kd->ecd", scaled_t, right_panel, preferred_element_type=jnp.float32)
        return summed * factor

    return per_device


def solution(mesh):
    placed = (P("eig", "basis"), P("basis", "chan"), P(), P("chan"), P(), P("basis"))
    return jax.shard_map(
        make_per_device(ring_order(mesh)),
        mesh=mesh,
        in_specs=placed,
        out_specs=P("basis", "chan", "eig"),
        check_vma=False,
    )
```

```python
import jax
import jax.numpy as jnp
import numpy as np
from jax import lax
from jax.sharding import PartitionSpec as P


def ring_order(mesh):
    n = mesh.shape["eig"]
    try:
        index = [0] * len(mesh.axis_names)
        where = mesh.axis_names.index("eig")
        coords = []
        for m in range(n):
            index[where] = m
            coords.append(tuple(int(v) for v in mesh.devices[tuple(index)].coords))
        varying = [a for a in range(len(coords[0])) if len({c[a] for c in coords}) > 1]
        if len(varying) != 2:
            return list(range(n))
        spans = [sorted({c[a] for c in coords}) for a in varying]
        if len(spans[0]) % 2 != 0:
            varying, spans = varying[::-1], spans[::-1]
        rows, cols = spans
        if len(rows) % 2 != 0 or len(cols) < 2 or len(rows) * len(cols) != n:
            return list(range(n))
        at = {(c[varying[0]], c[varying[1]]): m for m, c in enumerate(coords)}
        path = []
        for r_i, r in enumerate(rows):
            tail = cols[1:] if r_i % 2 == 0 else cols[1:][::-1]
            path += [at[(r, c)] for c in tail]
        path += [at[(r, cols[0])] for r in rows[::-1]]
        return path if sorted(path) == list(range(n)) else list(range(n))
    except Exception:
        return list(range(n))


def make_per_device(cycle, n_chan):
    n_ring = len(cycle)
    position = [0] * n_ring
    for t, m in enumerate(cycle):
        position[m] = t
    n_fwd = n_ring // 2
    long_pairs, short_pairs = [], []
    for j in range(n_chan):
        d = 1 if j % 2 == 0 else -1
        for t in range(n_ring):
            here = cycle[t] * n_chan + j
            long_pairs.append((here, cycle[(t + d) % n_ring] * n_chan + j))
            short_pairs.append((here, cycle[(t - d) % n_ring] * n_chan + j))
    n_bwd = n_ring - 1 - n_fwd

    def per_device(eigvecs, boundary, block_sizes, target_of_channel, poles, energies):
        n_eig = lax.axis_size("eig")
        rows_here = eigvecs.shape[1]
        block_ends = jnp.cumsum(block_sizes)
        row_ids = lax.axis_index("basis") * rows_here + jnp.arange(rows_here, dtype=jnp.int32)
        owner_of = jnp.sum((block_ends[None, :] <= row_ids[:, None]).astype(jnp.int32), axis=1)
        n_basis = lax.axis_size("basis")
        width = boundary.shape[1]
        halves = 2 if width % 256 == 0 else 1
        step = width // halves
        amp_parts = []
        for h in range(halves):
            cols = slice(h * step, (h + 1) * step)
            member = owner_of[:, None] == target_of_channel[None, cols]
            masked = jnp.where(member, boundary[:, cols], jnp.zeros_like(boundary[:, cols]))
            part = jnp.dot(eigvecs, masked, preferred_element_type=jnp.float32)
            total = part
            for s in range(1, n_basis):
                shift = [(b, (b + s) % n_basis) for b in range(n_basis)]
                total = total + lax.ppermute(part, "basis", shift)
            amp_parts.append(total.astype(jnp.bfloat16))
        amp = jnp.concatenate(amp_parts, axis=1) if halves > 1 else amp_parts[0]
        eig_index = lax.axis_index("eig")
        cycle_arr = jnp.array(cycle, dtype=jnp.int32)
        pos = jnp.array(position, dtype=jnp.int32)[eig_index]
        k_here = amp.shape[0]
        left_panel = jnp.zeros((k_here * n_ring, amp.shape[1]), amp.dtype)
        left_panel = lax.dynamic_update_slice_in_dim(left_panel, amp, eig_index * k_here, 0)
        sign = 1 - 2 * (lax.axis_index("chan") % 2)
        long_blk, short_blk = amp, amp
        for s in range(max(n_fwd, n_bwd)):
            if s < n_fwd:
                long_blk = lax.ppermute(long_blk, ("eig", "chan"), long_pairs)
                origin = cycle_arr[(pos - sign * (s + 1)) % n_ring]
                left_panel = lax.dynamic_update_slice_in_dim(left_panel, long_blk, origin * k_here, 0)
            if s < n_bwd:
                short_blk = lax.ppermute(short_blk, ("eig", "chan"), short_pairs)
                origin = cycle_arr[(pos + sign * (s + 1)) % n_ring]
                left_panel = lax.dynamic_update_slice_in_dim(left_panel, short_blk, origin * k_here, 0)
        own_width = left_panel.shape[1]
        col_width = own_width * n_chan // n_eig
        ratio = n_eig // n_chan
        piece = lax.dynamic_slice_in_dim(left_panel, (eig_index % ratio) * col_width, col_width, 1)
        holder = eig_index // ratio
        if n_chan == 2:
            other = lax.ppermute(piece, "chan", [(0, 1), (1, 0)])
            right_panel = jnp.where(lax.axis_index("chan") == holder, piece, other)
        else:
            pieces = lax.all_gather(piece, "chan", axis=0, tiled=False)
            right_panel = lax.dynamic_index_in_dim(pieces, holder, 0, keepdims=False)
        factor = poles.shape[0] ** (-0.5)
        weights = 1.0 / (poles[None, :] - energies[:, None])
        scaled = (weights[:, :, None] * left_panel[None].astype(jnp.float32)).astype(jnp.bfloat16)
        summed = jnp.einsum("ekc,kd->ecd", scaled, right_panel, preferred_element_type=jnp.float32)
        return summed * factor

    return per_device


def solution(mesh):
    placed = (P("eig", "basis"), P("basis", "chan"), P(), P("chan"), P(), P("basis"))
    return jax.shard_map(
        make_per_device(ring_order(mesh), mesh.shape["chan"]),
        mesh=mesh,
        in_specs=placed,
        out_specs=P("basis", "chan", "eig"),
        check_vma=False,
    )
```

```python
import jax
import jax.numpy as jnp
import numpy as np
from jax import lax
from jax.sharding import PartitionSpec as P


def ring_order(mesh):
    n = mesh.shape["eig"]
    try:
        index = [0] * len(mesh.axis_names)
        where = mesh.axis_names.index("eig")
        coords = []
        for m in range(n):
            index[where] = m
            coords.append(tuple(int(v) for v in mesh.devices[tuple(index)].coords))
        varying = [a for a in range(len(coords[0])) if len({c[a] for c in coords}) > 1]
        if len(varying) != 2:
            return list(range(n))
        spans = [sorted({c[a] for c in coords}) for a in varying]
        if len(spans[0]) % 2 != 0:
            varying, spans = varying[::-1], spans[::-1]
        rows, cols = spans
        if len(rows) % 2 != 0 or len(cols) < 2 or len(rows) * len(cols) != n:
            return list(range(n))
        at = {(c[varying[0]], c[varying[1]]): m for m, c in enumerate(coords)}
        path = []
        for r_i, r in enumerate(rows):
            tail = cols[1:] if r_i % 2 == 0 else cols[1:][::-1]
            path += [at[(r, c)] for c in tail]
        path += [at[(r, cols[0])] for r in rows[::-1]]
        return path if sorted(path) == list(range(n)) else list(range(n))
    except Exception:
        return list(range(n))


def make_per_device(cycle, n_chan):
    n_ring = len(cycle)
    position = [0] * n_ring
    for t, m in enumerate(cycle):
        position[m] = t
    n_fwd = n_ring // 2
    long_pairs, short_pairs = [], []
    for j in range(n_chan):
        d = 1 if j % 2 == 0 else -1
        for t in range(n_ring):
            here = cycle[t] * n_chan + j
            long_pairs.append((here, cycle[(t + d) % n_ring] * n_chan + j))
            short_pairs.append((here, cycle[(t - d) % n_ring] * n_chan + j))
    n_bwd = n_ring - 1 - n_fwd

    def per_device(eigvecs, boundary, block_sizes, target_of_channel, poles, energies):
        n_eig = lax.axis_size("eig")
        rows_here = eigvecs.shape[1]
        block_ends = jnp.cumsum(block_sizes)
        row_ids = lax.axis_index("basis") * rows_here + jnp.arange(rows_here, dtype=jnp.int32)
        owner_of = jnp.sum((block_ends[None, :] <= row_ids[:, None]).astype(jnp.int32), axis=1)
        n_basis = lax.axis_size("basis")
        width = boundary.shape[1]
        halves = 2 if width % 256 == 0 else 1
        step = width // halves
        amp_parts = []
        for h in range(halves):
            cols = slice(h * step, (h + 1) * step)
            member = owner_of[:, None] == target_of_channel[None, cols]
            masked = jnp.where(member, boundary[:, cols], jnp.zeros_like(boundary[:, cols]))
            part = jnp.dot(eigvecs, masked, preferred_element_type=jnp.float32)
            total = part
            for s in range(1, n_basis):
                shift = [(b, (b + s) % n_basis) for b in range(n_basis)]
                total = total + lax.ppermute(part, "basis", shift)
            amp_parts.append(total.astype(jnp.bfloat16))
        amp = jnp.concatenate(amp_parts, axis=1) if halves > 1 else amp_parts[0]
        eig_index = lax.axis_index("eig")
        cycle_arr = jnp.array(cycle, dtype=jnp.int32)
        pos = jnp.array(position, dtype=jnp.int32)[eig_index]
        k_here = amp.shape[0]
        left_panel = jnp.zeros((k_here * n_ring, amp.shape[1]), amp.dtype)
        left_panel = lax.dynamic_update_slice_in_dim(left_panel, amp, eig_index * k_here, 0)
        sign = 1 - 2 * (lax.axis_index("chan") % 2)
        n_split = 2 if amp.shape[1] % 256 == 0 else 1
        split_w = amp.shape[1] // n_split
        longs = [amp[:, p * split_w:(p + 1) * split_w] for p in range(n_split)]
        shorts = list(longs)
        for s in range(max(n_fwd, n_bwd)):
            if s < n_fwd:
                longs = [lax.ppermute(x, ("eig", "chan"), long_pairs) for x in longs]
                origin = cycle_arr[(pos - sign * (s + 1)) % n_ring]
                for p, x in enumerate(longs):
                    left_panel = lax.dynamic_update_slice(left_panel, x, (origin * k_here, p * split_w))
            if s < n_bwd:
                shorts = [lax.ppermute(x, ("eig", "chan"), short_pairs) for x in shorts]
                origin = cycle_arr[(pos + sign * (s + 1)) % n_ring]
                for p, x in enumerate(shorts):
                    left_panel = lax.dynamic_update_slice(left_panel, x, (origin * k_here, p * split_w))
        own_width = left_panel.shape[1]
        col_width = own_width * n_chan // n_eig
        ratio = n_eig // n_chan
        piece = lax.dynamic_slice_in_dim(left_panel, (eig_index % ratio) * col_width, col_width, 1)
        holder = eig_index // ratio
        if n_chan == 2:
            other = lax.ppermute(piece, "chan", [(0, 1), (1, 0)])
            right_panel = jnp.where(lax.axis_index("chan") == holder, piece, other)
        else:
            pieces = lax.all_gather(piece, "chan", axis=0, tiled=False)
            right_panel = lax.dynamic_index_in_dim(pieces, holder, 0, keepdims=False)
        factor = poles.shape[0] ** (-0.5)
        weights = 1.0 / (poles[None, :] - energies[:, None])
        scaled = (weights[:, :, None] * left_panel[None].astype(jnp.float32)).astype(jnp.bfloat16)
        summed = jnp.einsum("ekc,kd->ecd", scaled, right_panel, preferred_element_type=jnp.float32)
        return summed * factor

    return per_device


def solution(mesh):
    placed = (P("eig", "basis"), P("basis", "chan"), P(), P("chan"), P(), P("basis"))
    return jax.shard_map(
        make_per_device(ring_order(mesh), mesh.shape["chan"]),
        mesh=mesh,
        in_specs=placed,
        out_specs=P("basis", "chan", "eig"),
        check_vma=False,
    )
```

```python
import jax
import jax.numpy as jnp
import numpy as np
from jax import lax
from jax.sharding import PartitionSpec as P


def ring_order(mesh):
    n = mesh.shape["eig"]
    try:
        index = [0] * len(mesh.axis_names)
        where = mesh.axis_names.index("eig")
        coords = []
        for m in range(n):
            index[where] = m
            coords.append(tuple(int(v) for v in mesh.devices[tuple(index)].coords))
        varying = [a for a in range(len(coords[0])) if len({c[a] for c in coords}) > 1]
        if len(varying) != 2:
            return list(range(n))
        spans = [sorted({c[a] for c in coords}) for a in varying]
        if len(spans[0]) % 2 != 0:
            varying, spans = varying[::-1], spans[::-1]
        rows, cols = spans
        if len(rows) % 2 != 0 or len(cols) < 2 or len(rows) * len(cols) != n:
            return list(range(n))
        at = {(c[varying[0]], c[varying[1]]): m for m, c in enumerate(coords)}
        path = []
        for r_i, r in enumerate(rows):
            tail = cols[1:] if r_i % 2 == 0 else cols[1:][::-1]
            path += [at[(r, c)] for c in tail]
        path += [at[(r, cols[0])] for r in rows[::-1]]
        return path if sorted(path) == list(range(n)) else list(range(n))
    except Exception:
        return list(range(n))


def make_per_device(cycle, n_chan):
    n_ring = len(cycle)
    position = [0] * n_ring
    for t, m in enumerate(cycle):
        position[m] = t
    n_fwd = n_ring // 2
    long_pairs, short_pairs = [], []
    for j in range(n_chan):
        d = 1 if j % 2 == 0 else -1
        for t in range(n_ring):
            here = cycle[t] * n_chan + j
            long_pairs.append((here, cycle[(t + d) % n_ring] * n_chan + j))
            short_pairs.append((here, cycle[(t - d) % n_ring] * n_chan + j))
    n_bwd = n_ring - 1 - n_fwd

    def per_device(eigvecs, boundary, block_sizes, target_of_channel, poles, energies):
        n_eig = lax.axis_size("eig")
        rows_here = eigvecs.shape[1]
        block_ends = jnp.cumsum(block_sizes)
        row_ids = lax.axis_index("basis") * rows_here + jnp.arange(rows_here, dtype=jnp.int32)
        owner_of = jnp.sum((block_ends[None, :] <= row_ids[:, None]).astype(jnp.int32), axis=1)
        n_basis = lax.axis_size("basis")
        width = boundary.shape[1]
        halves = 4 if width % 512 == 0 else 1
        step = width // halves
        amp_parts = []
        for h in range(halves):
            cols = slice(h * step, (h + 1) * step)
            member = owner_of[:, None] == target_of_channel[None, cols]
            masked = jnp.where(member, boundary[:, cols], jnp.zeros_like(boundary[:, cols]))
            part = jnp.dot(eigvecs, masked, preferred_element_type=jnp.float32)
            total = part
            for s in range(1, n_basis):
                shift = [(b, (b + s) % n_basis) for b in range(n_basis)]
                total = total + lax.ppermute(part, "basis", shift)
            amp_parts.append(total.astype(jnp.bfloat16))
        eig_index = lax.axis_index("eig")
        cycle_arr = jnp.array(cycle, dtype=jnp.int32)
        pos = jnp.array(position, dtype=jnp.int32)[eig_index]
        k_here = amp_parts[0].shape[0]
        left_panel = jnp.zeros((k_here * n_ring, width), jnp.bfloat16)
        for p, x in enumerate(amp_parts):
            left_panel = lax.dynamic_update_slice(left_panel, x, (eig_index * k_here, p * step))
        sign = 1 - 2 * (lax.axis_index("chan") % 2)
        split_w = step
        longs = list(amp_parts)
        shorts = list(amp_parts)
        for s in range(max(n_fwd, n_bwd)):
            if s < n_fwd:
                longs = [lax.ppermute(x, ("eig", "chan"), long_pairs) for x in longs]
                origin = cycle_arr[(pos - sign * (s + 1)) % n_ring]
                for p, x in enumerate(longs):
                    left_panel = lax.dynamic_update_slice(left_panel, x, (origin * k_here, p * split_w))
            if s < n_bwd:
                shorts = [lax.ppermute(x, ("eig", "chan"), short_pairs) for x in shorts]
                origin = cycle_arr[(pos + sign * (s + 1)) % n_ring]
                for p, x in enumerate(shorts):
                    left_panel = lax.dynamic_update_slice(left_panel, x, (origin * k_here, p * split_w))
        own_width = left_panel.shape[1]
        col_width = own_width * n_chan // n_eig
        ratio = n_eig // n_chan
        piece = lax.dynamic_slice_in_dim(left_panel, (eig_index % ratio) * col_width, col_width, 1)
        holder = eig_index // ratio
        if n_chan == 2:
            other = lax.ppermute(piece, "chan", [(0, 1), (1, 0)])
            right_panel = jnp.where(lax.axis_index("chan") == holder, piece, other)
        else:
            pieces = lax.all_gather(piece, "chan", axis=0, tiled=False)
            right_panel = lax.dynamic_index_in_dim(pieces, holder, 0, keepdims=False)
        factor = poles.shape[0] ** (-0.5)
        weights = 1.0 / (poles[None, :] - energies[:, None])
        scaled = (weights[:, :, None] * left_panel[None].astype(jnp.float32)).astype(jnp.bfloat16)
        summed = jnp.einsum("ekc,kd->ecd", scaled, right_panel, preferred_element_type=jnp.float32)
        return summed * factor

    return per_device


def solution(mesh):
    placed = (P("eig", "basis"), P("basis", "chan"), P(), P("chan"), P(), P("basis"))
    return jax.shard_map(
        make_per_device(ring_order(mesh), mesh.shape["chan"]),
        mesh=mesh,
        in_specs=placed,
        out_specs=P("basis", "chan", "eig"),
        check_vma=False,
    )
```

```python
import jax
import jax.numpy as jnp
import numpy as np
from jax import lax
from jax.sharding import PartitionSpec as P


def ring_order(mesh):
    n = mesh.shape["eig"]
    try:
        index = [0] * len(mesh.axis_names)
        where = mesh.axis_names.index("eig")
        coords = []
        for m in range(n):
            index[where] = m
            coords.append(tuple(int(v) for v in mesh.devices[tuple(index)].coords))
        varying = [a for a in range(len(coords[0])) if len({c[a] for c in coords}) > 1]
        if len(varying) != 2:
            return list(range(n))
        spans = [sorted({c[a] for c in coords}) for a in varying]
        if len(spans[0]) % 2 != 0:
            varying, spans = varying[::-1], spans[::-1]
        rows, cols = spans
        if len(rows) % 2 != 0 or len(cols) < 2 or len(rows) * len(cols) != n:
            return list(range(n))
        at = {(c[varying[0]], c[varying[1]]): m for m, c in enumerate(coords)}
        path = []
        for r_i, r in enumerate(rows):
            tail = cols[1:] if r_i % 2 == 0 else cols[1:][::-1]
            path += [at[(r, c)] for c in tail]
        path += [at[(r, cols[0])] for r in rows[::-1]]
        return path if sorted(path) == list(range(n)) else list(range(n))
    except Exception:
        return list(range(n))


def make_per_device(cycle, n_chan):
    n_ring = len(cycle)
    position = [0] * n_ring
    for t, m in enumerate(cycle):
        position[m] = t
    n_fwd = n_ring // 2
    long_pairs, short_pairs = [], []
    for j in range(n_chan):
        d = 1 if j % 2 == 0 else -1
        for t in range(n_ring):
            here = cycle[t] * n_chan + j
            long_pairs.append((here, cycle[(t + d) % n_ring] * n_chan + j))
            short_pairs.append((here, cycle[(t - d) % n_ring] * n_chan + j))
    n_bwd = n_ring - 1 - n_fwd

    def per_device(eigvecs, boundary, block_sizes, target_of_channel, poles, energies):
        n_eig = lax.axis_size("eig")
        rows_here = eigvecs.shape[1]
        block_ends = jnp.cumsum(block_sizes)
        row_ids = lax.axis_index("basis") * rows_here + jnp.arange(rows_here, dtype=jnp.int32)
        owner_of = jnp.sum((block_ends[None, :] <= row_ids[:, None]).astype(jnp.int32), axis=1)
        n_basis = lax.axis_size("basis")
        width = boundary.shape[1]
        eig_index = lax.axis_index("eig")
        cycle_arr = jnp.array(cycle, dtype=jnp.int32)
        pos = jnp.array(position, dtype=jnp.int32)[eig_index]
        sign = 1 - 2 * (lax.axis_index("chan") % 2)
        k_here = eigvecs.shape[0]
        left_panel = jnp.zeros((k_here * n_ring, width), jnp.bfloat16)
        halves = 2 if width % 256 == 0 else 1
        step = width // halves
        parts = []
        for h in range(halves):
            cols = slice(h * step, (h + 1) * step)
            member = owner_of[:, None] == target_of_channel[None, cols]
            masked = jnp.where(member, boundary[:, cols], jnp.zeros_like(boundary[:, cols]))
            parts.append(jnp.dot(eigvecs, masked, preferred_element_type=jnp.float32))
        if n_basis == 2 and halves == 2:
            mine = lax.axis_index("basis")
            swap = [(0, 1), (1, 0)]
            keep = jnp.where(mine == 0, parts[0], parts[1])
            give = jnp.where(mine == 0, parts[1], parts[0])
            amp_mine = (keep + lax.ppermute(give, "basis", swap)).astype(jnp.bfloat16)
            own_col = mine * step
            other_col = (1 - mine) * step
            left_panel = lax.dynamic_update_slice(left_panel, amp_mine, (eig_index * k_here, own_col))
            got = lax.ppermute(amp_mine, "basis", swap)
            left_panel = lax.dynamic_update_slice(left_panel, got, (eig_index * k_here, other_col))
            long_blk, short_blk = amp_mine, amp_mine
            for s in range(max(n_fwd, n_bwd)):
                new_blocks = []
                if s < n_fwd:
                    long_blk = lax.ppermute(long_blk, ("eig", "chan"), long_pairs)
                    origin = cycle_arr[(pos - sign * (s + 1)) % n_ring]
                    left_panel = lax.dynamic_update_slice(left_panel, long_blk, (origin * k_here, own_col))
                    new_blocks.append((long_blk, origin))
                if s < n_bwd:
                    short_blk = lax.ppermute(short_blk, ("eig", "chan"), short_pairs)
                    origin = cycle_arr[(pos + sign * (s + 1)) % n_ring]
                    left_panel = lax.dynamic_update_slice(left_panel, short_blk, (origin * k_here, own_col))
                    new_blocks.append((short_blk, origin))
                sent = jnp.concatenate([b for b, _ in new_blocks], axis=0)
                got = lax.ppermute(sent, "basis", swap)
                for i, (_, origin) in enumerate(new_blocks):
                    piece_i = got[i * k_here:(i + 1) * k_here]
                    left_panel = lax.dynamic_update_slice(left_panel, piece_i, (origin * k_here, other_col))
        else:
            amp_parts = []
            for part in parts:
                total = part
                for s in range(1, n_basis):
                    shift = [(b, (b + s) % n_basis) for b in range(n_basis)]
                    total = total + lax.ppermute(part, "basis", shift)
                amp_parts.append(total.astype(jnp.bfloat16))
            for p, x in enumerate(amp_parts):
                left_panel = lax.dynamic_update_slice(left_panel, x, (eig_index * k_here, p * step))
            longs = list(amp_parts)
            shorts = list(amp_parts)
            for s in range(max(n_fwd, n_bwd)):
                if s < n_fwd:
                    longs = [lax.ppermute(x, ("eig", "chan"), long_pairs) for x in longs]
                    origin = cycle_arr[(pos - sign * (s + 1)) % n_ring]
                    for p, x in enumerate(longs):
                        left_panel = lax.dynamic_update_slice(left_panel, x, (origin * k_here, p * step))
                if s < n_bwd:
                    shorts = [lax.ppermute(x, ("eig", "chan"), short_pairs) for x in shorts]
                    origin = cycle_arr[(pos + sign * (s + 1)) % n_ring]
                    for p, x in enumerate(shorts):
                        left_panel = lax.dynamic_update_slice(left_panel, x, (origin * k_here, p * step))
        own_width = left_panel.shape[1]
        col_width = own_width * n_chan // n_eig
        ratio = n_eig // n_chan
        piece = lax.dynamic_slice_in_dim(left_panel, (eig_index % ratio) * col_width, col_width, 1)
        holder = eig_index // ratio
        if n_chan == 2:
            other = lax.ppermute(piece, "chan", [(0, 1), (1, 0)])
            right_panel = jnp.where(lax.axis_index("chan") == holder, piece, other)
        else:
            pieces = lax.all_gather(piece, "chan", axis=0, tiled=False)
            right_panel = lax.dynamic_index_in_dim(pieces, holder, 0, keepdims=False)
        factor = poles.shape[0] ** (-0.5)
        weights = 1.0 / (poles[None, :] - energies[:, None])
        scaled = (weights[:, :, None] * left_panel[None].astype(jnp.float32)).astype(jnp.bfloat16)
        summed = jnp.einsum("ekc,kd->ecd", scaled, right_panel, preferred_element_type=jnp.float32)
        return summed * factor

    return per_device


def solution(mesh):
    placed = (P("eig", "basis"), P("basis", "chan"), P(), P("chan"), P(), P("basis"))
    return jax.shard_map(
        make_per_device(ring_order(mesh), mesh.shape["chan"]),
        mesh=mesh,
        in_specs=placed,
        out_specs=P("basis", "chan", "eig"),
        check_vma=False,
    )
```

```python
import jax
import jax.numpy as jnp
import numpy as np
from jax import lax
from jax.sharding import PartitionSpec as P


def ring_order(mesh):
    n = mesh.shape["eig"]
    try:
        index = [0] * len(mesh.axis_names)
        where = mesh.axis_names.index("eig")
        coords = []
        for m in range(n):
            index[where] = m
            coords.append(tuple(int(v) for v in mesh.devices[tuple(index)].coords))
        varying = [a for a in range(len(coords[0])) if len({c[a] for c in coords}) > 1]
        if len(varying) != 2:
            return list(range(n))
        spans = [sorted({c[a] for c in coords}) for a in varying]
        if len(spans[0]) % 2 != 0:
            varying, spans = varying[::-1], spans[::-1]
        rows, cols = spans
        if len(rows) % 2 != 0 or len(cols) < 2 or len(rows) * len(cols) != n:
            return list(range(n))
        at = {(c[varying[0]], c[varying[1]]): m for m, c in enumerate(coords)}
        path = []
        for r_i, r in enumerate(rows):
            tail = cols[1:] if r_i % 2 == 0 else cols[1:][::-1]
            path += [at[(r, c)] for c in tail]
        path += [at[(r, cols[0])] for r in rows[::-1]]
        return path if sorted(path) == list(range(n)) else list(range(n))
    except Exception:
        return list(range(n))


def make_per_device(cycle, n_chan):
    n_ring = len(cycle)
    position = [0] * n_ring
    for t, m in enumerate(cycle):
        position[m] = t
    n_fwd = n_ring // 2
    long_pairs, short_pairs = [], []
    for j in range(n_chan):
        d = 1 if j % 2 == 0 else -1
        for t in range(n_ring):
            here = cycle[t] * n_chan + j
            long_pairs.append((here, cycle[(t + d) % n_ring] * n_chan + j))
            short_pairs.append((here, cycle[(t - d) % n_ring] * n_chan + j))
    n_bwd = n_ring - 1 - n_fwd

    def per_device(eigvecs, boundary, block_sizes, target_of_channel, poles, energies):
        n_eig = lax.axis_size("eig")
        rows_here = eigvecs.shape[1]
        block_ends = jnp.cumsum(block_sizes)
        row_ids = lax.axis_index("basis") * rows_here + jnp.arange(rows_here, dtype=jnp.int32)
        owner_of = jnp.sum((block_ends[None, :] <= row_ids[:, None]).astype(jnp.int32), axis=1)
        n_basis = lax.axis_size("basis")
        width = boundary.shape[1]
        eig_index = lax.axis_index("eig")
        cycle_arr = jnp.array(cycle, dtype=jnp.int32)
        pos = jnp.array(position, dtype=jnp.int32)[eig_index]
        sign = 1 - 2 * (lax.axis_index("chan") % 2)
        k_here = eigvecs.shape[0]
        left_panel = jnp.zeros((k_here * n_ring, width), jnp.bfloat16)
        halves = 2 if width % 256 == 0 else 1
        step = width // halves
        parts = []
        for h in range(halves):
            cols = slice(h * step, (h + 1) * step)
            member = owner_of[:, None] == target_of_channel[None, cols]
            masked = jnp.where(member, boundary[:, cols], jnp.zeros_like(boundary[:, cols]))
            parts.append(jnp.dot(eigvecs, masked, preferred_element_type=jnp.float32))
        if n_basis == 2 and halves == 2:
            mine = lax.axis_index("basis")
            swap = [(0, 1), (1, 0)]
            keep = jnp.where(mine == 0, parts[0], parts[1])
            give = jnp.where(mine == 0, parts[1], parts[0])
            amp_mine = (keep + lax.ppermute(give, "basis", swap)).astype(jnp.bfloat16)
            own_half = jnp.zeros((k_here * n_ring, step), jnp.bfloat16)
            other_half = jnp.zeros((k_here * n_ring, step), jnp.bfloat16)
            own_half = lax.dynamic_update_slice_in_dim(own_half, amp_mine, eig_index * k_here, 0)
            got = lax.ppermute(amp_mine, "basis", swap)
            other_half = lax.dynamic_update_slice_in_dim(other_half, got, eig_index * k_here, 0)
            long_blk, short_blk = amp_mine, amp_mine
            for s in range(max(n_fwd, n_bwd)):
                new_blocks = []
                if s < n_fwd:
                    long_blk = lax.ppermute(long_blk, ("eig", "chan"), long_pairs)
                    origin = cycle_arr[(pos - sign * (s + 1)) % n_ring]
                    own_half = lax.dynamic_update_slice_in_dim(own_half, long_blk, origin * k_here, 0)
                    new_blocks.append((long_blk, origin))
                if s < n_bwd:
                    short_blk = lax.ppermute(short_blk, ("eig", "chan"), short_pairs)
                    origin = cycle_arr[(pos + sign * (s + 1)) % n_ring]
                    own_half = lax.dynamic_update_slice_in_dim(own_half, short_blk, origin * k_here, 0)
                    new_blocks.append((short_blk, origin))
                sent = jnp.concatenate([blk for blk, _ in new_blocks], axis=0)
                got = lax.ppermute(sent, "basis", swap)
                for i, (_, origin) in enumerate(new_blocks):
                    piece_i = got[i * k_here:(i + 1) * k_here]
                    other_half = lax.dynamic_update_slice_in_dim(other_half, piece_i, origin * k_here, 0)
            first = mine == 0
            left_panel = jnp.concatenate(
                [jnp.where(first, own_half, other_half), jnp.where(first, other_half, own_half)], axis=1
            )
        else:
            amp_parts = []
            for part in parts:
                total = part
                for s in range(1, n_basis):
                    shift = [(b, (b + s) % n_basis) for b in range(n_basis)]
                    total = total + lax.ppermute(part, "basis", shift)
                amp_parts.append(total.astype(jnp.bfloat16))
            for p, x in enumerate(amp_parts):
                left_panel = lax.dynamic_update_slice(left_panel, x, (eig_index * k_here, p * step))
            longs = list(amp_parts)
            shorts = list(amp_parts)
            for s in range(max(n_fwd, n_bwd)):
                if s < n_fwd:
                    longs = [lax.ppermute(x, ("eig", "chan"), long_pairs) for x in longs]
                    origin = cycle_arr[(pos - sign * (s + 1)) % n_ring]
                    for p, x in enumerate(longs):
                        left_panel = lax.dynamic_update_slice(left_panel, x, (origin * k_here, p * step))
                if s < n_bwd:
                    shorts = [lax.ppermute(x, ("eig", "chan"), short_pairs) for x in shorts]
                    origin = cycle_arr[(pos + sign * (s + 1)) % n_ring]
                    for p, x in enumerate(shorts):
                        left_panel = lax.dynamic_update_slice(left_panel, x, (origin * k_here, p * step))
        own_width = left_panel.shape[1]
        col_width = own_width * n_chan // n_eig
        ratio = n_eig // n_chan
        piece = lax.dynamic_slice_in_dim(left_panel, (eig_index % ratio) * col_width, col_width, 1)
        holder = eig_index // ratio
        if n_chan == 2:
            other = lax.ppermute(piece, "chan", [(0, 1), (1, 0)])
            right_panel = jnp.where(lax.axis_index("chan") == holder, piece, other)
        else:
            pieces = lax.all_gather(piece, "chan", axis=0, tiled=False)
            right_panel = lax.dynamic_index_in_dim(pieces, holder, 0, keepdims=False)
        factor = poles.shape[0] ** (-0.5)
        weights = 1.0 / (poles[None, :] - energies[:, None])
        scaled = (weights[:, :, None] * left_panel[None].astype(jnp.float32)).astype(jnp.bfloat16)
        summed = jnp.einsum("ekc,kd->ecd", scaled, right_panel, preferred_element_type=jnp.float32)
        return summed * factor

    return per_device


def solution(mesh):
    placed = (P("eig", "basis"), P("basis", "chan"), P(), P("chan"), P(), P("basis"))
    return jax.shard_map(
        make_per_device(ring_order(mesh), mesh.shape["chan"]),
        mesh=mesh,
        in_specs=placed,
        out_specs=P("basis", "chan", "eig"),
        check_vma=False,
    )
```

```python
import jax
import jax.numpy as jnp
import numpy as np
from jax import lax
from jax.sharding import PartitionSpec as P


def ring_order(mesh):
    n = mesh.shape["eig"]
    try:
        index = [0] * len(mesh.axis_names)
        where = mesh.axis_names.index("eig")
        coords = []
        for m in range(n):
            index[where] = m
            coords.append(tuple(int(v) for v in mesh.devices[tuple(index)].coords))
        varying = [a for a in range(len(coords[0])) if len({c[a] for c in coords}) > 1]
        if len(varying) != 2:
            return list(range(n))
        spans = [sorted({c[a] for c in coords}) for a in varying]
        if len(spans[0]) % 2 != 0:
            varying, spans = varying[::-1], spans[::-1]
        rows, cols = spans
        if len(rows) % 2 != 0 or len(cols) < 2 or len(rows) * len(cols) != n:
            return list(range(n))
        at = {(c[varying[0]], c[varying[1]]): m for m, c in enumerate(coords)}
        path = []
        for r_i, r in enumerate(rows):
            tail = cols[1:] if r_i % 2 == 0 else cols[1:][::-1]
            path += [at[(r, c)] for c in tail]
        path += [at[(r, cols[0])] for r in rows[::-1]]
        return path if sorted(path) == list(range(n)) else list(range(n))
    except Exception:
        return list(range(n))


def make_per_device(cycle, n_chan):
    n_ring = len(cycle)
    position = [0] * n_ring
    for t, m in enumerate(cycle):
        position[m] = t
    n_fwd = n_ring // 2
    long_pairs, short_pairs = [], []
    for j in range(n_chan):
        d = 1 if j % 2 == 0 else -1
        for t in range(n_ring):
            here = cycle[t] * n_chan + j
            long_pairs.append((here, cycle[(t + d) % n_ring] * n_chan + j))
            short_pairs.append((here, cycle[(t - d) % n_ring] * n_chan + j))
    n_bwd = n_ring - 1 - n_fwd

    def per_device(eigvecs, boundary, block_sizes, target_of_channel, poles, energies):
        n_eig = lax.axis_size("eig")
        rows_here = eigvecs.shape[1]
        n_blocks = block_sizes.shape[0]
        upto = jnp.arange(n_blocks)[:, None] >= jnp.arange(n_blocks)[None, :]
        block_ends = jnp.sum(jnp.where(upto, block_sizes[None, :], 0), axis=1)
        row_ids = lax.axis_index("basis") * rows_here + jnp.arange(rows_here, dtype=jnp.int32)
        owner_of = jnp.sum((block_ends[None, :] <= row_ids[:, None]).astype(jnp.int32), axis=1)
        n_basis = lax.axis_size("basis")
        width = boundary.shape[1]
        halves = 2 if width % 256 == 0 else 1
        step = width // halves
        amp_parts = []
        for h in range(halves):
            cols = slice(h * step, (h + 1) * step)
            member = owner_of[:, None] == target_of_channel[None, cols]
            masked = jnp.where(member, boundary[:, cols], jnp.zeros_like(boundary[:, cols]))
            part = jnp.dot(eigvecs, masked, preferred_element_type=jnp.float32)
            total = part
            for s in range(1, n_basis):
                shift = [(b, (b + s) % n_basis) for b in range(n_basis)]
                total = total + lax.ppermute(part, "basis", shift)
            amp_parts.append(total.astype(jnp.bfloat16))
        amp = jnp.concatenate(amp_parts, axis=1) if halves > 1 else amp_parts[0]
        eig_index = lax.axis_index("eig")
        cycle_arr = jnp.array(cycle, dtype=jnp.int32)
        pos = jnp.array(position, dtype=jnp.int32)[eig_index]
        k_here = amp.shape[0]
        left_panel = jnp.zeros((k_here * n_ring, amp.shape[1]), amp.dtype)
        left_panel = lax.dynamic_update_slice_in_dim(left_panel, amp, eig_index * k_here, 0)
        sign = 1 - 2 * (lax.axis_index("chan") % 2)
        n_split = 2 if amp.shape[1] % 256 == 0 else 1
        split_w = amp.shape[1] // n_split
        longs = [amp[:, p * split_w:(p + 1) * split_w] for p in range(n_split)]
        shorts = list(longs)
        for s in range(max(n_fwd, n_bwd)):
            if s < n_fwd:
                longs = [lax.ppermute(x, ("eig", "chan"), long_pairs) for x in longs]
                origin = cycle_arr[(pos - sign * (s + 1)) % n_ring]
                for p, x in enumerate(longs):
                    left_panel = lax.dynamic_update_slice(left_panel, x, (origin * k_here, p * split_w))
            if s < n_bwd:
                shorts = [lax.ppermute(x, ("eig", "chan"), short_pairs) for x in shorts]
                origin = cycle_arr[(pos + sign * (s + 1)) % n_ring]
                for p, x in enumerate(shorts):
                    left_panel = lax.dynamic_update_slice(left_panel, x, (origin * k_here, p * split_w))
        own_width = left_panel.shape[1]
        col_width = own_width * n_chan // n_eig
        ratio = n_eig // n_chan
        piece = lax.dynamic_slice_in_dim(left_panel, (eig_index % ratio) * col_width, col_width, 1)
        holder = eig_index // ratio
        if n_chan == 2:
            other = lax.ppermute(piece, "chan", [(0, 1), (1, 0)])
            right_panel = jnp.where(lax.axis_index("chan") == holder, piece, other)
        else:
            pieces = lax.all_gather(piece, "chan", axis=0, tiled=False)
            right_panel = lax.dynamic_index_in_dim(pieces, holder, 0, keepdims=False)
        factor = poles.shape[0] ** (-0.5)
        weights = 1.0 / (poles[None, :] - energies[:, None])
        scaled = (weights[:, :, None] * left_panel[None].astype(jnp.float32)).astype(jnp.bfloat16)
        summed = jnp.einsum("ekc,kd->ecd", scaled, right_panel, preferred_element_type=jnp.float32)
        return summed * factor

    return per_device


def solution(mesh):
    placed = (P("eig", "basis"), P("basis", "chan"), P(), P("chan"), P(), P("basis"))
    return jax.shard_map(
        make_per_device(ring_order(mesh), mesh.shape["chan"]),
        mesh=mesh,
        in_specs=placed,
        out_specs=P("basis", "chan", "eig"),
        check_vma=False,
    )
```

```python
import jax
import jax.numpy as jnp
import numpy as np
from jax import lax
from jax.sharding import PartitionSpec as P


def ring_order(mesh):
    n = mesh.shape["eig"]
    try:
        index = [0] * len(mesh.axis_names)
        where = mesh.axis_names.index("eig")
        coords = []
        for m in range(n):
            index[where] = m
            coords.append(tuple(int(v) for v in mesh.devices[tuple(index)].coords))
        varying = [a for a in range(len(coords[0])) if len({c[a] for c in coords}) > 1]
        if len(varying) != 2:
            return list(range(n))
        spans = [sorted({c[a] for c in coords}) for a in varying]
        if len(spans[0]) % 2 != 0:
            varying, spans = varying[::-1], spans[::-1]
        rows, cols = spans
        if len(rows) % 2 != 0 or len(cols) < 2 or len(rows) * len(cols) != n:
            return list(range(n))
        at = {(c[varying[0]], c[varying[1]]): m for m, c in enumerate(coords)}
        path = []
        for r_i, r in enumerate(rows):
            tail = cols[1:] if r_i % 2 == 0 else cols[1:][::-1]
            path += [at[(r, c)] for c in tail]
        path += [at[(r, cols[0])] for r in rows[::-1]]
        return path if sorted(path) == list(range(n)) else list(range(n))
    except Exception:
        return list(range(n))


def make_per_device(cycle, n_chan):
    n_ring = len(cycle)
    position = [0] * n_ring
    for t, m in enumerate(cycle):
        position[m] = t
    n_fwd = n_ring // 2
    long_pairs, short_pairs = [], []
    for j in range(n_chan):
        d = 1 if j % 2 == 0 else -1
        for t in range(n_ring):
            here = cycle[t] * n_chan + j
            long_pairs.append((here, cycle[(t + d) % n_ring] * n_chan + j))
            short_pairs.append((here, cycle[(t - d) % n_ring] * n_chan + j))
    n_bwd = n_ring - 1 - n_fwd

    def per_device(eigvecs, boundary, block_sizes, target_of_channel, poles, energies):
        n_eig = lax.axis_size("eig")
        rows_here = eigvecs.shape[1]
        n_blocks = block_sizes.shape[0]
        upto = jnp.arange(n_blocks)[:, None] >= jnp.arange(n_blocks)[None, :]
        block_ends = jnp.sum(jnp.where(upto, block_sizes[None, :], 0), axis=1)
        row_ids = lax.axis_index("basis") * rows_here + jnp.arange(rows_here, dtype=jnp.int32)
        owner_of = jnp.sum((block_ends[None, :] <= row_ids[:, None]).astype(jnp.int32), axis=1)
        n_basis = lax.axis_size("basis")
        width = boundary.shape[1]
        halves = 2 if width % 256 == 0 else 1
        step = width // halves
        amp_parts = []
        for h in range(halves):
            cols = slice(h * step, (h + 1) * step)
            member = owner_of[:, None] == target_of_channel[None, cols]
            masked = jnp.where(member, boundary[:, cols], jnp.zeros_like(boundary[:, cols]))
            part = jnp.dot(eigvecs, masked, preferred_element_type=jnp.float32)
            total = part
            for s in range(1, n_basis):
                shift = [(b, (b + s) % n_basis) for b in range(n_basis)]
                total = total + lax.ppermute(part, "basis", shift)
            amp_parts.append(total.astype(jnp.bfloat16))
        eig_index = lax.axis_index("eig")
        cycle_arr = jnp.array(cycle, dtype=jnp.int32)
        pos = jnp.array(position, dtype=jnp.int32)[eig_index]
        k_here = amp_parts[0].shape[0]
        left_panel = jnp.zeros((k_here * n_ring, width), jnp.bfloat16)
        left_panel = lax.dynamic_update_slice(left_panel, amp_parts[0], (eig_index * k_here, 0))
        sign = 1 - 2 * (lax.axis_index("chan") % 2)
        split_w = step
        longs = list(amp_parts)
        shorts = list(amp_parts)
        for s in range(max(n_fwd, n_bwd)):
            if s < n_fwd:
                longs = [lax.ppermute(x, ("eig", "chan"), long_pairs) for x in longs]
                origin = cycle_arr[(pos - sign * (s + 1)) % n_ring]
                for p, x in enumerate(longs):
                    left_panel = lax.dynamic_update_slice(left_panel, x, (origin * k_here, p * split_w))
            if s < n_bwd:
                shorts = [lax.ppermute(x, ("eig", "chan"), short_pairs) for x in shorts]
                origin = cycle_arr[(pos + sign * (s + 1)) % n_ring]
                for p, x in enumerate(shorts):
                    left_panel = lax.dynamic_update_slice(left_panel, x, (origin * k_here, p * split_w))
        for p, x in enumerate(amp_parts[1:]):
            left_panel = lax.dynamic_update_slice(left_panel, x, (eig_index * k_here, (p + 1) * step))
        own_width = left_panel.shape[1]
        col_width = own_width * n_chan // n_eig
        ratio = n_eig // n_chan
        piece = lax.dynamic_slice_in_dim(left_panel, (eig_index % ratio) * col_width, col_width, 1)
        holder = eig_index // ratio
        if n_chan == 2:
            other = lax.ppermute(piece, "chan", [(0, 1), (1, 0)])
            right_panel = jnp.where(lax.axis_index("chan") == holder, piece, other)
        else:
            pieces = lax.all_gather(piece, "chan", axis=0, tiled=False)
            right_panel = lax.dynamic_index_in_dim(pieces, holder, 0, keepdims=False)
        factor = poles.shape[0] ** (-0.5)
        weights = 1.0 / (poles[None, :] - energies[:, None])
        scaled = (weights[:, :, None] * left_panel[None].astype(jnp.float32)).astype(jnp.bfloat16)
        summed = jnp.einsum("ekc,kd->ecd", scaled, right_panel, preferred_element_type=jnp.float32)
        return summed * factor

    return per_device


def solution(mesh):
    placed = (P("eig", "basis"), P("basis", "chan"), P(), P("chan"), P(), P("basis"))
    return jax.shard_map(
        make_per_device(ring_order(mesh), mesh.shape["chan"]),
        mesh=mesh,
        in_specs=placed,
        out_specs=P("basis", "chan", "eig"),
        check_vma=False,
    )
```

```python
import jax
import jax.numpy as jnp
import numpy as np
from jax import lax
from jax.sharding import PartitionSpec as P


def ring_order(mesh):
    n = mesh.shape["eig"]
    try:
        index = [0] * len(mesh.axis_names)
        where = mesh.axis_names.index("eig")
        coords = []
        for m in range(n):
            index[where] = m
            coords.append(tuple(int(v) for v in mesh.devices[tuple(index)].coords))
        varying = [a for a in range(len(coords[0])) if len({c[a] for c in coords}) > 1]
        if len(varying) != 2:
            return list(range(n))
        spans = [sorted({c[a] for c in coords}) for a in varying]
        if len(spans[0]) % 2 != 0:
            varying, spans = varying[::-1], spans[::-1]
        rows, cols = spans
        if len(rows) % 2 != 0 or len(cols) < 2 or len(rows) * len(cols) != n:
            return list(range(n))
        at = {(c[varying[0]], c[varying[1]]): m for m, c in enumerate(coords)}
        path = []
        for r_i, r in enumerate(rows):
            tail = cols[1:] if r_i % 2 == 0 else cols[1:][::-1]
            path += [at[(r, c)] for c in tail]
        path += [at[(r, cols[0])] for r in rows[::-1]]
        return path if sorted(path) == list(range(n)) else list(range(n))
    except Exception:
        return list(range(n))


def make_per_device(cycle, n_chan):
    n_ring = len(cycle)
    position = [0] * n_ring
    for t, m in enumerate(cycle):
        position[m] = t
    n_fwd = n_ring // 2
    long_pairs, short_pairs = [], []
    for j in range(n_chan):
        d = 1 if j % 2 == 0 else -1
        for t in range(n_ring):
            here = cycle[t] * n_chan + j
            long_pairs.append((here, cycle[(t + d) % n_ring] * n_chan + j))
            short_pairs.append((here, cycle[(t - d) % n_ring] * n_chan + j))
    n_bwd = n_ring - 1 - n_fwd

    def per_device(eigvecs, boundary, block_sizes, target_of_channel, poles, energies):
        n_eig = lax.axis_size("eig")
        rows_here = eigvecs.shape[1]
        n_blocks = block_sizes.shape[0]
        upto = jnp.arange(n_blocks)[:, None] >= jnp.arange(n_blocks)[None, :]
        block_ends = jnp.sum(jnp.where(upto, block_sizes[None, :], 0), axis=1)
        row_ids = lax.axis_index("basis") * rows_here + jnp.arange(rows_here, dtype=jnp.int32)
        owner_of = jnp.sum((block_ends[None, :] <= row_ids[:, None]).astype(jnp.int32), axis=1)
        n_basis = lax.axis_size("basis")
        width = boundary.shape[1]
        halves = 2 if width % 256 == 0 else 1
        step = width // halves
        amp_parts = []
        for h in range(halves):
            cols = slice(h * step, (h + 1) * step)
            member = owner_of[:, None] == target_of_channel[None, cols]
            masked = jnp.where(member, boundary[:, cols], jnp.zeros_like(boundary[:, cols]))
            part = jnp.dot(eigvecs, masked, preferred_element_type=jnp.float32)
            if n_basis == 2 and part.shape[0] % 16 == 0:
                rows = part.shape[0] // 2
                mine = lax.axis_index("basis")
                keep = lax.dynamic_slice_in_dim(part, mine * rows, rows, 0)
                give = lax.dynamic_slice_in_dim(part, (1 - mine) * rows, rows, 0)
                summed = (keep + lax.ppermute(give, "basis", [(0, 1), (1, 0)])).astype(jnp.bfloat16)
                other = lax.ppermute(summed, "basis", [(0, 1), (1, 0)])
                first = mine == 0
                upper = jnp.where(first, summed, other)
                lower = jnp.where(first, other, summed)
                amp_parts.append(jnp.concatenate([upper, lower], axis=0))
                continue
            total = part
            for s in range(1, n_basis):
                shift = [(b, (b + s) % n_basis) for b in range(n_basis)]
                total = total + lax.ppermute(part, "basis", shift)
            amp_parts.append(total.astype(jnp.bfloat16))
        amp = jnp.concatenate(amp_parts, axis=1) if halves > 1 else amp_parts[0]
        eig_index = lax.axis_index("eig")
        cycle_arr = jnp.array(cycle, dtype=jnp.int32)
        pos = jnp.array(position, dtype=jnp.int32)[eig_index]
        k_here = amp.shape[0]
        left_panel = jnp.zeros((k_here * n_ring, amp.shape[1]), amp.dtype)
        left_panel = lax.dynamic_update_slice_in_dim(left_panel, amp, eig_index * k_here, 0)
        sign = 1 - 2 * (lax.axis_index("chan") % 2)
        n_split = 2 if amp.shape[1] % 256 == 0 else 1
        split_w = amp.shape[1] // n_split
        longs = [amp[:, p * split_w:(p + 1) * split_w] for p in range(n_split)]
        shorts = list(longs)
        for s in range(max(n_fwd, n_bwd)):
            if s < n_fwd:
                longs = [lax.ppermute(x, ("eig", "chan"), long_pairs) for x in longs]
                origin = cycle_arr[(pos - sign * (s + 1)) % n_ring]
                for p, x in enumerate(longs):
                    left_panel = lax.dynamic_update_slice(left_panel, x, (origin * k_here, p * split_w))
            if s < n_bwd:
                shorts = [lax.ppermute(x, ("eig", "chan"), short_pairs) for x in shorts]
                origin = cycle_arr[(pos + sign * (s + 1)) % n_ring]
                for p, x in enumerate(shorts):
                    left_panel = lax.dynamic_update_slice(left_panel, x, (origin * k_here, p * split_w))
        own_width = left_panel.shape[1]
        col_width = own_width * n_chan // n_eig
        ratio = n_eig // n_chan
        piece = lax.dynamic_slice_in_dim(left_panel, (eig_index % ratio) * col_width, col_width, 1)
        holder = eig_index // ratio
        if n_chan == 2:
            other = lax.ppermute(piece, "chan", [(0, 1), (1, 0)])
            right_panel = jnp.where(lax.axis_index("chan") == holder, piece, other)
        else:
            pieces = lax.all_gather(piece, "chan", axis=0, tiled=False)
            right_panel = lax.dynamic_index_in_dim(pieces, holder, 0, keepdims=False)
        factor = poles.shape[0] ** (-0.5)
        weights = 1.0 / (poles[None, :] - energies[:, None])
        scaled = (weights[:, :, None] * left_panel[None].astype(jnp.float32)).astype(jnp.bfloat16)
        summed = jnp.einsum("ekc,kd->ecd", scaled, right_panel, preferred_element_type=jnp.float32)
        return summed * factor

    return per_device


def solution(mesh):
    placed = (P("eig", "basis"), P("basis", "chan"), P(), P("chan"), P(), P("basis"))
    return jax.shard_map(
        make_per_device(ring_order(mesh), mesh.shape["chan"]),
        mesh=mesh,
        in_specs=placed,
        out_specs=P("basis", "chan", "eig"),
        check_vma=False,
    )
```

```python
import jax
import jax.numpy as jnp
import numpy as np
from jax import lax
from jax.sharding import PartitionSpec as P


def ring_order(mesh):
    n = mesh.shape["eig"]
    try:
        index = [0] * len(mesh.axis_names)
        where = mesh.axis_names.index("eig")
        coords = []
        for m in range(n):
            index[where] = m
            coords.append(tuple(int(v) for v in mesh.devices[tuple(index)].coords))
        varying = [a for a in range(len(coords[0])) if len({c[a] for c in coords}) > 1]
        if len(varying) != 2:
            return list(range(n))
        spans = [sorted({c[a] for c in coords}) for a in varying]
        if len(spans[0]) % 2 != 0:
            varying, spans = varying[::-1], spans[::-1]
        rows, cols = spans
        if len(rows) % 2 != 0 or len(cols) < 2 or len(rows) * len(cols) != n:
            return list(range(n))
        at = {(c[varying[0]], c[varying[1]]): m for m, c in enumerate(coords)}
        path = []
        for r_i, r in enumerate(rows):
            tail = cols[1:] if r_i % 2 == 0 else cols[1:][::-1]
            path += [at[(r, c)] for c in tail]
        path += [at[(r, cols[0])] for r in rows[::-1]]
        return path if sorted(path) == list(range(n)) else list(range(n))
    except Exception:
        return list(range(n))


def make_per_device(cycle, n_chan):
    n_ring = len(cycle)
    position = [0] * n_ring
    for t, m in enumerate(cycle):
        position[m] = t
    n_fwd = n_ring // 2
    long_pairs, short_pairs = [], []
    for j in range(n_chan):
        d = 1 if j % 2 == 0 else -1
        for t in range(n_ring):
            here = cycle[t] * n_chan + j
            long_pairs.append((here, cycle[(t + d) % n_ring] * n_chan + j))
            short_pairs.append((here, cycle[(t - d) % n_ring] * n_chan + j))
    n_bwd = n_ring - 1 - n_fwd

    def per_device(eigvecs, boundary, block_sizes, target_of_channel, poles, energies):
        n_eig = lax.axis_size("eig")
        rows_here = eigvecs.shape[1]
        n_blocks = block_sizes.shape[0]
        upto = jnp.arange(n_blocks)[:, None] >= jnp.arange(n_blocks)[None, :]
        block_ends = jnp.sum(jnp.where(upto, block_sizes[None, :], 0), axis=1)
        row_ids = lax.axis_index("basis") * rows_here + jnp.arange(rows_here, dtype=jnp.int32)
        owner_of = jnp.sum((block_ends[None, :] <= row_ids[:, None]).astype(jnp.int32), axis=1)
        n_basis = lax.axis_size("basis")
        width = boundary.shape[1]
        halves = 2 if width % 256 == 0 else 1
        step = width // halves
        amp_parts = []
        for h in range(halves):
            cols = slice(h * step, (h + 1) * step)
            member = owner_of[:, None] == target_of_channel[None, cols]
            masked = jnp.where(member, boundary[:, cols], jnp.zeros_like(boundary[:, cols]))
            part = jnp.dot(eigvecs, masked, preferred_element_type=jnp.float32)
            total = part
            for s in range(1, n_basis):
                shift = [(b, (b + s) % n_basis) for b in range(n_basis)]
                total = total + lax.ppermute(part, "basis", shift)
            amp_parts.append(total.astype(jnp.bfloat16))
        amp = jnp.concatenate(amp_parts, axis=1) if halves > 1 else amp_parts[0]
        eig_index = lax.axis_index("eig")
        cycle_arr = jnp.array(cycle, dtype=jnp.int32)
        pos = jnp.array(position, dtype=jnp.int32)[eig_index]
        k_here = amp.shape[0]
        left_panel = jnp.zeros((k_here * n_ring, amp.shape[1]), amp.dtype)
        left_panel = lax.dynamic_update_slice_in_dim(left_panel, amp, eig_index * k_here, 0)
        sign = 1 - 2 * (lax.axis_index("chan") % 2)
        n_split = 2 if amp.shape[1] % 256 == 0 else 1
        split_w = amp.shape[1] // n_split
        tag = jnp.full((8, 128), eig_index, jnp.float32)
        long_from = lax.ppermute(tag, ("eig", "chan"), long_pairs)[0, 0].astype(jnp.int32)
        short_from = lax.ppermute(tag, ("eig", "chan"), short_pairs)[0, 0].astype(jnp.int32)
        longs = [amp[:, p * split_w:(p + 1) * split_w] for p in range(n_split)]
        shorts = list(longs)
        for s in range(max(n_fwd, n_bwd)):
            if s < n_fwd:
                longs = [lax.ppermute(x, ("eig", "chan"), long_pairs) for x in longs]
                origin = long_from if s == 0 else cycle_arr[(pos - sign * (s + 1)) % n_ring]
                for p, x in enumerate(longs):
                    left_panel = lax.dynamic_update_slice(left_panel, x, (origin * k_here, p * split_w))
            if s < n_bwd:
                shorts = [lax.ppermute(x, ("eig", "chan"), short_pairs) for x in shorts]
                origin = short_from if s == 0 else cycle_arr[(pos + sign * (s + 1)) % n_ring]
                for p, x in enumerate(shorts):
                    left_panel = lax.dynamic_update_slice(left_panel, x, (origin * k_here, p * split_w))
        own_width = left_panel.shape[1]
        col_width = own_width * n_chan // n_eig
        ratio = n_eig // n_chan
        piece = lax.dynamic_slice_in_dim(left_panel, (eig_index % ratio) * col_width, col_width, 1)
        holder = eig_index // ratio
        if n_chan == 2:
            other = lax.ppermute(piece, "chan", [(0, 1), (1, 0)])
            right_panel = jnp.where(lax.axis_index("chan") == holder, piece, other)
        else:
            pieces = lax.all_gather(piece, "chan", axis=0, tiled=False)
            right_panel = lax.dynamic_index_in_dim(pieces, holder, 0, keepdims=False)
        factor = poles.shape[0] ** (-0.5)
        weights = 1.0 / (poles[None, :] - energies[:, None])
        scaled = (weights[:, :, None] * left_panel[None].astype(jnp.float32)).astype(jnp.bfloat16)
        summed = jnp.einsum("ekc,kd->ecd", scaled, right_panel, preferred_element_type=jnp.float32)
        return summed * factor

    return per_device


def solution(mesh):
    placed = (P("eig", "basis"), P("basis", "chan"), P(), P("chan"), P(), P("basis"))
    return jax.shard_map(
        make_per_device(ring_order(mesh), mesh.shape["chan"]),
        mesh=mesh,
        in_specs=placed,
        out_specs=P("basis", "chan", "eig"),
        check_vma=False,
    )
```

```python
import jax
import jax.numpy as jnp
import numpy as np
from jax import lax
from jax.sharding import PartitionSpec as P


def ring_order(mesh):
    n = mesh.shape["eig"]
    try:
        index = [0] * len(mesh.axis_names)
        where = mesh.axis_names.index("eig")
        coords = []
        for m in range(n):
            index[where] = m
            coords.append(tuple(int(v) for v in mesh.devices[tuple(index)].coords))
        varying = [a for a in range(len(coords[0])) if len({c[a] for c in coords}) > 1]
        if len(varying) != 2:
            return list(range(n))
        spans = [sorted({c[a] for c in coords}) for a in varying]
        if len(spans[0]) % 2 != 0:
            varying, spans = varying[::-1], spans[::-1]
        rows, cols = spans
        if len(rows) % 2 != 0 or len(cols) < 2 or len(rows) * len(cols) != n:
            return list(range(n))
        at = {(c[varying[0]], c[varying[1]]): m for m, c in enumerate(coords)}
        path = []
        for r_i, r in enumerate(rows):
            tail = cols[1:] if r_i % 2 == 0 else cols[1:][::-1]
            path += [at[(r, c)] for c in tail]
        path += [at[(r, cols[0])] for r in rows[::-1]]
        return path if sorted(path) == list(range(n)) else list(range(n))
    except Exception:
        return list(range(n))


def make_per_device(cycle, n_chan):
    n_ring = len(cycle)
    position = [0] * n_ring
    for t, m in enumerate(cycle):
        position[m] = t
    n_fwd = n_ring // 2
    long_pairs, short_pairs = [], []
    for j in range(n_chan):
        d = 1 if j % 2 == 0 else -1
        for t in range(n_ring):
            here = cycle[t] * n_chan + j
            long_pairs.append((here, cycle[(t + d) % n_ring] * n_chan + j))
            short_pairs.append((here, cycle[(t - d) % n_ring] * n_chan + j))
    n_bwd = n_ring - 1 - n_fwd

    def per_device(eigvecs, boundary, block_sizes, target_of_channel, poles, energies):
        n_eig = lax.axis_size("eig")
        rows_here = eigvecs.shape[1]
        n_blocks = block_sizes.shape[0]
        upto = jnp.arange(n_blocks)[:, None] >= jnp.arange(n_blocks)[None, :]
        block_ends = jnp.sum(jnp.where(upto, block_sizes[None, :], 0), axis=1)
        row_ids = lax.axis_index("basis") * rows_here + jnp.arange(rows_here, dtype=jnp.int32)
        owner_of = jnp.sum((block_ends[None, :] <= row_ids[:, None]).astype(jnp.int32), axis=1)
        n_basis = lax.axis_size("basis")
        width = boundary.shape[1]
        halves = 2 if width % 256 == 0 else 1
        step = width // halves
        amp_parts = []
        for h in range(halves):
            cols = slice(h * step, (h + 1) * step)
            member = owner_of[:, None] == target_of_channel[None, cols]
            masked = jnp.where(member, boundary[:, cols], jnp.zeros_like(boundary[:, cols]))
            part = jnp.dot(eigvecs, masked, preferred_element_type=jnp.float32)
            total = part
            for s in range(1, n_basis):
                shift = [(b, (b + s) % n_basis) for b in range(n_basis)]
                total = total + lax.ppermute(part, "basis", shift)
            amp_parts.append(total.astype(jnp.bfloat16))
        amp = jnp.concatenate(amp_parts, axis=1) if halves > 1 else amp_parts[0]
        eig_index = lax.axis_index("eig")
        cycle_arr = jnp.array(cycle, dtype=jnp.int32)
        pos = jnp.array(position, dtype=jnp.int32)[eig_index]
        k_here = amp.shape[0]
        left_panel = jnp.zeros((k_here * n_ring, amp.shape[1]), amp.dtype)
        left_panel = lax.dynamic_update_slice_in_dim(left_panel, amp, eig_index * k_here, 0)
        sign = 1 - 2 * (lax.axis_index("chan") % 2)
        n_split = 2 if amp.shape[1] % 256 == 0 else 1
        split_w = amp.shape[1] // n_split
        longs = [amp[:, p * split_w:(p + 1) * split_w] for p in range(n_split)]
        shorts = [amp]
        for s in range(max(n_fwd, n_bwd)):
            if s < n_fwd:
                longs = [lax.ppermute(x, ("eig", "chan"), long_pairs) for x in longs]
                origin = cycle_arr[(pos - sign * (s + 1)) % n_ring]
                for p, x in enumerate(longs):
                    left_panel = lax.dynamic_update_slice(left_panel, x, (origin * k_here, p * split_w))
            if s < n_bwd:
                shorts = [lax.ppermute(x, ("eig", "chan"), short_pairs) for x in shorts]
                origin = cycle_arr[(pos + sign * (s + 1)) % n_ring]
                for x in shorts:
                    left_panel = lax.dynamic_update_slice(left_panel, x, (origin * k_here, 0))
        own_width = left_panel.shape[1]
        col_width = own_width * n_chan // n_eig
        ratio = n_eig // n_chan
        piece = lax.dynamic_slice_in_dim(left_panel, (eig_index % ratio) * col_width, col_width, 1)
        holder = eig_index // ratio
        if n_chan == 2:
            other = lax.ppermute(piece, "chan", [(0, 1), (1, 0)])
            right_panel = jnp.where(lax.axis_index("chan") == holder, piece, other)
        else:
            pieces = lax.all_gather(piece, "chan", axis=0, tiled=False)
            right_panel = lax.dynamic_index_in_dim(pieces, holder, 0, keepdims=False)
        factor = poles.shape[0] ** (-0.5)
        weights = 1.0 / (poles[None, :] - energies[:, None])
        scaled = (weights[:, :, None] * left_panel[None].astype(jnp.float32)).astype(jnp.bfloat16)
        summed = jnp.einsum("ekc,kd->ecd", scaled, right_panel, preferred_element_type=jnp.float32)
        return summed * factor

    return per_device


def solution(mesh):
    placed = (P("eig", "basis"), P("basis", "chan"), P(), P("chan"), P(), P("basis"))
    return jax.shard_map(
        make_per_device(ring_order(mesh), mesh.shape["chan"]),
        mesh=mesh,
        in_specs=placed,
        out_specs=P("basis", "chan", "eig"),
        check_vma=False,
    )
```
